256 devices in a mesh: wave: 64 (over z, y, core), lev: 4 (over x).
Axes of the slice: x: 4, y: 4, z: 8, core: 2. Of those that a mesh axis runs over, the one named last changes fastest.
Arguments:
- coefficients: bfloat16 [640, 2, 128, 640], P('wave', None, 'lev'), may hold values from -0.1796875 to 0.1796875
- legendre: bfloat16 [640, 2, 640, 512], P('wave'), may hold values from -0.25 to 0.25
- pair_wave: int32 [640], replicated, may hold values from 0 to 639, each once
- row_points: int32 [512], replicated, may hold values from 20 to 5136, as said below
- layer_logpressure_factor: float32 [16], replicated, may hold values from 0.05 to 0.5
Outputs:
- physical_space_values: bfloat16 [1024, 64, 5248], P('wave', 'lev')
- geopotential: bfloat16 [1024, 16, 5248], P('wave', 'lev')
The draws below stay inside these ranges and needn't reach their ends.
Inputs may be any that keep to these rules, and one draw needn't show every extreme that they name: Pair q holds zonal wavenumbers pair_wave[q] and 1279 - pair_wave[q]; each value appears once. `row_points`: the northern rows from the pole toward the equator: 16 + 4 j points for distinct octahedral rows j of 1 to 1280, strictly rising; the last row is j = 1280.
All inputs are finite; a program needn't handle non-finite values.
Results may differ from the reference program's by a relative error of at most 0.0062.
Values may be sent and summed in bfloat16 or wider, within the bound.
No kernel may reach another device: no remote copies, remote signals or barrier semaphores. Data moves between devices by JAX's collectives and lax.ppermute only.
A program may use at most 128 MiB of HBM per device.

```python
import math
import jax
import jax.numpy as jnp
from jax import lax

TRUNC = 1279
KH = 640
PAIRS = 640
NLAT = 1024
NLATH = 512
LEV = 16
QUANTITY_COUNT = 4
LF = 64
LCAP = 5248


def draw_row_points(key, part):
    row_order = jax.random.permutation(key, TRUNC)
    chosen = jnp.sort(row_order[:NLATH - 1]).astype(jnp.int32) + 1
    row_numbers = jnp.concatenate([chosen, jnp.array([TRUNC + 1], jnp.int32)])
    return (16 + 4 * row_numbers).astype(jnp.int32)


def steps_of(stream_key, shape, shards, least, high):
    def one(axis_at, shards_of):
        steps = jax.random.uniform(jax.random.fold_in(jax.random.fold_in(stream_key, 6), axis_at), (shards_of,), jnp.float32, least / len(shards), high / len(shards))
        return jnp.repeat(jnp.exp(steps), shape[axis_at] // shards_of).reshape((-1,) + (1,) * (len(shape) - axis_at - 1))

    gain = one(*shards[0])
    for cut in shards[1:]:
        gain = gain * one(*cut)
    return gain


def normal_values(stream_key, dims, scale, reach, split=(), held_as=jnp.bfloat16):
    values = scale * jax.random.normal(stream_key, dims, jnp.float32)
    if split:
        values = values * steps_of(stream_key, dims, split, -0.22, 0.18)
    return jnp.clip(values, -reach, reach).astype(held_as)


def setup_inputs(seed: int = 0) -> dict:
    streams_of = jax.random.split(jax.random.key(seed), 6)
    return {
        "coefficients": normal_values(streams_of[0], (PAIRS, 2, 2 * LF, KH), 0.03, 0.1796875, ((0, 64), (2, 4))),
        "legendre": normal_values(streams_of[1], (PAIRS, 2, KH, NLATH), KH ** -0.5, 0.25, ((0, 64),)),
        "pair_wave": jax.random.permutation(streams_of[2], PAIRS).astype(jnp.int32),
        "row_points": draw_row_points(jax.random.fold_in(streams_of[5], 71), 0),
        "layer_logpressure_factor": jnp.clip(jnp.exp(jax.random.uniform(streams_of[4], (LEV,), jnp.float32, math.log(0.05), math.log(0.5))), 0.05, 0.5),
    }


two_pi = 6.283185307179586


def pair_masks(low_waves, pack_width):
    parity = jnp.arange(2, dtype=jnp.int32)
    low_count = (TRUNC - low_waves[:, None] - parity[None, :]) // 2 + 1
    high_count = (low_waves[:, None] - parity[None, :]) // 2 + 1
    pack_index = jnp.arange(pack_width, dtype=jnp.int32)[None, None, :]
    low_mask = pack_index < low_count[:, :, None]
    high_mask = (pack_index >= low_count[:, :, None]) & (pack_index < (low_count + high_count)[:, :, None])
    return jnp.stack([low_mask, high_mask], axis=2)


def angle_of(residue, points):
    return residue.astype(jnp.float32) * (jnp.float32(two_pi) / points.astype(jnp.float32))


def synth_row(fourier_row, points, wave_numbers):
    fields = fourier_row.shape[0]
    wave_limit = jnp.minimum(TRUNC, (points - 1) // 2)
    kept_coef = fourier_row * (wave_numbers <= wave_limit).astype(jnp.float32)[None, None, :]
    real_part = kept_coef[:, 0, :]
    imag_part = kept_coef[:, 1, :]
    offsets = jnp.arange(128, dtype=jnp.int32)
    base_angle = angle_of((wave_numbers[:, None] * offsets[None, :]) % points, points)
    base_table = jnp.concatenate([jnp.cos(base_angle), -jnp.sin(base_angle)], axis=0).astype(jnp.bfloat16)
    blocks = (points + 127) // 128

    def block_step(block_index, row_out):
        block_shift = (128 * block_index) % points
        twist = angle_of((wave_numbers * block_shift) % points, points)
        twist_cos = jnp.cos(twist)
        twist_sin = jnp.sin(twist)
        twisted = jnp.concatenate([real_part * twist_cos - imag_part * twist_sin,
                                   real_part * twist_sin + imag_part * twist_cos], axis=1).astype(jnp.bfloat16)
        block_values = jnp.dot(twisted, base_table, preferred_element_type=jnp.float32)
        position = 128 * block_index + offsets
        block_values = jnp.where(position[None, :] < points, block_values, 0.0)
        return lax.dynamic_update_slice_in_dim(row_out, block_values.astype(jnp.bfloat16), 128 * block_index, 1)

    return lax.fori_loop(0, blocks, block_step, jnp.zeros((fields, LCAP), jnp.bfloat16))


def legendre_pair(pair_pack):
    coef_pair, table_pair, mask_pair = pair_pack
    selected = coef_pair[:, None, :, :] * mask_pair[:, :, None, :].astype(jnp.bfloat16)
    legendre_sums = jnp.einsum("ehck,ekt->ethc", selected.astype(jnp.float32), table_pair.astype(jnp.float32),
                               precision=lax.Precision.HIGHEST)
    north_rows = legendre_sums[0] + legendre_sums[1]
    south_rows = jnp.flip(legendre_sums[0] - legendre_sums[1], 0)
    return jnp.concatenate([north_rows, south_rows], 0)


def reference(coefficients, legendre, pair_wave, row_points, layer_logpressure_factor):
    selection = pair_masks(pair_wave, KH)
    legendre_all = lax.map(legendre_pair, (coefficients, legendre, selection))
    fourier = jnp.transpose(legendre_all.reshape(PAIRS, NLAT, 2, LF, 2), (1, 3, 4, 0, 2)).reshape(NLAT, LF, 2, 2 * PAIRS)
    wave_numbers = jnp.stack([pair_wave, TRUNC - pair_wave], axis=1).reshape(-1).astype(jnp.int32)
    points_all = jnp.concatenate([row_points, jnp.flip(row_points)]).astype(jnp.int32)

    def one_row(row_pack):
        return synth_row(row_pack[0], row_pack[1], wave_numbers)

    physical_space_values = lax.map(one_row, (fourier, points_all))
    heat_state_values = physical_space_values[:, 0::QUANTITY_COUNT, :].astype(jnp.float32)
    scaled_heat_values = heat_state_values * layer_logpressure_factor[None, :, None]
    underlying_partial_totals = jnp.flip(jnp.cumsum(jnp.flip(scaled_heat_values, 1), axis=1), 1)
    return physical_space_values, underlying_partial_totals.astype(jnp.bfloat16)
```

```python
import jax
import jax.numpy as jnp
from jax import lax
from jax.sharding import PartitionSpec as P

TRUNC = 1279
QUANTITY_COUNT = 4
LCAP = 5248
BLOCK = 128
BLOCKS = LCAP // BLOCK

two_pi = 6.283185307179586


def pair_masks(low_waves, pack_width):
    parity = jnp.arange(2, dtype=jnp.int32)
    low_count = (TRUNC - low_waves[:, None] - parity[None, :]) // 2 + 1
    high_count = (low_waves[:, None] - parity[None, :]) // 2 + 1
    pack_index = jnp.arange(pack_width, dtype=jnp.int32)[None, None, :]
    low_mask = pack_index < low_count[:, :, None]
    high_mask = (pack_index >= low_count[:, :, None]) & (
        pack_index < (low_count + high_count)[:, :, None]
    )
    return jnp.stack([low_mask, high_mask], axis=2)


def residue(j, points):
    q = jnp.floor(j.astype(jnp.float32) / points.astype(jnp.float32)).astype(jnp.int32)
    r = j - q * points
    r = jnp.where(r < 0, r + points, r)
    return jnp.where(r >= points, r - points, r)


def phase(waves, steps, points):
    j = waves * steps
    rem = residue(j, points)
    angle = rem.astype(jnp.float32) * (jnp.float32(two_pi) / points.astype(jnp.float32))
    return jnp.cos(angle), jnp.sin(angle)


def times(a, b):
    return a[0] * b[0] - a[1] * b[1], a[1] * b[0] + a[0] * b[1]


def tables(wave_numbers, lengths):
    rows = lengths.shape[0]
    slots = wave_numbers.shape[0]
    w = wave_numbers[None, None, :]
    pts = lengths[:, None, None]
    low = phase(w, jnp.arange(16, dtype=jnp.int32)[None, :, None], pts)
    high = phase(w, 16 * jnp.arange(8, dtype=jnp.int32)[None, :, None], pts)
    cos_b, sin_b = times(
        (high[0][:, :, None, :], high[1][:, :, None, :]),
        (low[0][:, None, :, :], low[1][:, None, :, :]),
    )
    base_t = jnp.concatenate(
        [cos_b.reshape(rows, BLOCK, slots), -sin_b.reshape(rows, BLOCK, slots)], axis=2
    ).astype(jnp.bfloat16)
    near = phase(w, BLOCK * jnp.arange(8, dtype=jnp.int32)[None, :, None], pts)
    far = phase(w, 8 * BLOCK * jnp.arange(6, dtype=jnp.int32)[None, :, None], pts)
    cos_t, sin_t = times(
        (far[0][:, :, None, :], far[1][:, :, None, :]),
        (near[0][:, None, :, :], near[1][:, None, :, :]),
    )
    wave_limit = jnp.minimum(TRUNC, (lengths - 1) // 2)
    keep = (wave_numbers[None, :] <= wave_limit[:, None]).astype(jnp.float32)[:, None, :]
    cos_t = cos_t.reshape(rows, 48, slots)[:, :BLOCKS] * keep
    sin_t = sin_t.reshape(rows, 48, slots)[:, :BLOCKS] * keep
    return base_t, cos_t, sin_t


def synth_row(pack):
    fourier_row, base_t, cos_t, sin_t, points = pack
    fields = fourier_row.shape[0] // 2
    real_part = fourier_row[:fields]
    imag_part = fourier_row[fields:]
    c = cos_t[:, None, :]
    s = sin_t[:, None, :]
    twisted = jnp.concatenate(
        [real_part[None] * c - imag_part[None] * s, real_part[None] * s + imag_part[None] * c],
        axis=2,
    ).astype(jnp.bfloat16)
    values = jnp.einsum("bfs,ks->fbk", twisted, base_t, preferred_element_type=jnp.float32)
    values = values.reshape(fields, LCAP)
    position = jnp.arange(LCAP, dtype=jnp.int32)
    values = jnp.where(position[None, :] < points, values, 0.0)
    return values.astype(jnp.bfloat16)


def local(coefficients, legendre, pair_wave, row_points, layer_logpressure_factor):
    wave_count = lax.axis_size("wave")
    wave_rank = lax.axis_index("wave")
    pair_local, _, cols, pack_width = coefficients.shape
    fields = cols // 2
    half_rows = legendre.shape[3]
    all_rows = 2 * half_rows
    band_rows = all_rows // wave_count
    half_bands = half_rows // band_rows
    my_pairs = lax.dynamic_slice_in_dim(pair_wave, wave_rank * pair_local, pair_local)
    selection = pair_masks(my_pairs, pack_width).astype(jnp.bfloat16)
    coef = coefficients.reshape(pair_local, 2, fields, 2, pack_width).transpose(0, 1, 3, 2, 4)
    coef = coef.reshape(pair_local, 2, cols, pack_width)
    selected = coef[:, :, None, :, :] * selection[:, :, :, None, :]
    signs = jnp.array([[1.0, 1.0], [1.0, -1.0]], jnp.bfloat16)
    lhs = signs[None, :, :, None, None, None] * selected[:, None]
    sums = jnp.einsum("qaehci,qeit->atqhc", lhs, legendre, preferred_element_type=jnp.float32)
    sums = sums.reshape(2, half_bands, band_rows, pair_local * 2, cols)
    south = jnp.flip(sums[1], (0, 1))
    bands = jnp.concatenate([sums[0], south], 0)
    send = bands.transpose(0, 2, 1, 3).reshape(wave_count, pair_local * 2, band_rows * cols)
    got = lax.all_to_all(send, "wave", 0, 0, tiled=True)
    slots = got.shape[0] * got.shape[1]
    fourier = got.reshape(slots, band_rows * cols).T.reshape(band_rows, cols, slots)

    wave_numbers = jnp.stack([pair_wave, TRUNC - pair_wave], axis=1).reshape(-1)
    points_all = jnp.concatenate([row_points, jnp.flip(row_points)])
    lengths = lax.dynamic_slice_in_dim(points_all, wave_rank * band_rows, band_rows)
    base_t, cos_t, sin_t = tables(wave_numbers, lengths)
    values = lax.map(synth_row, (fourier, base_t, cos_t, sin_t, lengths), batch_size=4)

    heat_state_values = values[:, 0::QUANTITY_COUNT, :].astype(jnp.float32)
    device_layers = heat_state_values.shape[1]
    lev_rank = lax.axis_index("lev")
    layer_depth_factor = lax.dynamic_slice_in_dim(
        layer_logpressure_factor, lev_rank * device_layers, device_layers
    )
    scaled_heat_values = heat_state_values * layer_depth_factor[None, :, None]
    partial_totals = jnp.flip(jnp.cumsum(jnp.flip(scaled_heat_values, 1), axis=1), 1)
    everything = lax.all_gather(partial_totals[:, 0, :], "lev")
    lev_count = everything.shape[0]
    below = (jnp.arange(lev_count) > lev_rank).astype(jnp.float32)[:, None, None]
    deeper = jnp.sum(everything * below, axis=0)
    geopotential = (partial_totals + deeper[:, None, :]).astype(jnp.bfloat16)
    return (values, geopotential)


def solution(mesh):
    return jax.shard_map(
        local,
        mesh=mesh,
        in_specs=(P("wave", None, "lev", None), P("wave", None, None, None), P(), P(), P()),
        out_specs=(P("wave", "lev", None), P("wave", "lev", None)),
        check_vma=False,
    )
```

```python
import jax
import jax.numpy as jnp
from jax import lax
from jax.sharding import PartitionSpec as P
from jax.experimental import pallas as pl
from jax.experimental.pallas import tpu as pltpu

TRUNC = 1279
QUANTITY_COUNT = 4
LCAP = 5248
BLOCK = 128
BLOCKS = LCAP // BLOCK

two_pi = 6.283185307179586


def pair_masks(low_waves, pack_width):
    parity = jnp.arange(2, dtype=jnp.int32)
    low_count = (TRUNC - low_waves[:, None] - parity[None, :]) // 2 + 1
    high_count = (low_waves[:, None] - parity[None, :]) // 2 + 1
    pack_index = jnp.arange(pack_width, dtype=jnp.int32)[None, None, :]
    low_mask = pack_index < low_count[:, :, None]
    high_mask = (pack_index >= low_count[:, :, None]) & (
        pack_index < (low_count + high_count)[:, :, None]
    )
    return jnp.stack([low_mask, high_mask], axis=2)


def residue(j, points):
    q = jnp.floor(j.astype(jnp.float32) / points.astype(jnp.float32)).astype(jnp.int32)
    r = j - q * points
    r = jnp.where(r < 0, r + points, r)
    return jnp.where(r >= points, r - points, r)


def phase(waves, steps, points):
    j = waves * steps
    rem = residue(j, points)
    angle = rem.astype(jnp.float32) * (jnp.float32(two_pi) / points.astype(jnp.float32))
    return jnp.cos(angle), jnp.sin(angle)


def times(a, b):
    return a[0] * b[0] - a[1] * b[1], a[1] * b[0] + a[0] * b[1]


def tables(wave_numbers, lengths):
    rows = lengths.shape[0]
    slots = wave_numbers.shape[0]
    w = wave_numbers[None, None, :]
    pts = lengths[:, None, None]
    low = phase(w, jnp.arange(16, dtype=jnp.int32)[None, :, None], pts)
    high = phase(w, 16 * jnp.arange(8, dtype=jnp.int32)[None, :, None], pts)
    cos_b, sin_b = times(
        (high[0][:, :, None, :], high[1][:, :, None, :]),
        (low[0][:, None, :, :], low[1][:, None, :, :]),
    )
    base_t = jnp.concatenate(
        [cos_b.reshape(rows, BLOCK, slots), -sin_b.reshape(rows, BLOCK, slots)], axis=2
    ).astype(jnp.bfloat16)
    near = phase(w, BLOCK * jnp.arange(8, dtype=jnp.int32)[None, :, None], pts)
    far = phase(w, 8 * BLOCK * jnp.arange(6, dtype=jnp.int32)[None, :, None], pts)
    cos_t, sin_t = times(
        (far[0][:, :, None, :], far[1][:, :, None, :]),
        (near[0][:, None, :, :], near[1][:, None, :, :]),
    )
    wave_limit = jnp.minimum(TRUNC, (lengths - 1) // 2)
    keep = (wave_numbers[None, :] <= wave_limit[:, None]).astype(jnp.float32)[:, None, :]
    live = (jnp.arange(48) < BLOCKS).astype(jnp.float32)[None, :, None] * keep
    cos_t = cos_t.reshape(rows, 48, slots) * live
    sin_t = sin_t.reshape(rows, 48, slots) * live
    return base_t, cos_t, sin_t


def main_kernel(lengths_ref, rowmap_ref, f_ref, base_ref, cos_ref, sin_ref, out_ref, tw_ref):
    r = pl.program_id(0)
    points = lengths_ref[r]
    fields = out_ref.shape[1]
    slots = f_ref.shape[2]
    real_part = f_ref[0, 0:fields, :]
    imag_part = f_ref[0, fields:2 * fields, :]
    for b in range(BLOCKS):
        c = cos_ref[0, b:b + 1, :]
        s = sin_ref[0, b:b + 1, :]
        rows = slice(fields * b, fields * (b + 1))
        tw_ref[rows, 0:slots] = (real_part * c - imag_part * s).astype(jnp.bfloat16)
        tw_ref[rows, slots:2 * slots] = (real_part * s + imag_part * c).astype(jnp.bfloat16)
    values = lax.dot_general(tw_ref[...], base_ref[0], (((1,), (1,)), ((), ())),
                             preferred_element_type=jnp.float32)
    lane = lax.broadcasted_iota(jnp.int32, (fields, BLOCK), 1)
    for b in range(BLOCKS):
        v = values[fields * b:fields * (b + 1), :]
        v = jnp.where(lane + BLOCK * b < points, v, 0.0)
        out_ref[0, :, BLOCK * b:BLOCK * (b + 1)] = v.astype(jnp.bfloat16)


def heat_kernel(lengths_ref, rowmap_ref, f_ref, base_ref, cos_ref, sin_ref, out_ref, tw_ref):
    r = pl.program_id(0)
    points = lengths_ref[r]
    fields = out_ref.shape[1]
    slots = f_ref.shape[2]
    depth = cos_ref.shape[1]
    c = cos_ref[0]
    s = sin_ref[0]
    for f in range(fields):
        re = f_ref[0, f:f + 1, :]
        im = f_ref[0, fields + f:fields + f + 1, :]
        rows = slice(depth * f, depth * (f + 1))
        tw_ref[rows, 0:slots] = (re * c - im * s).astype(jnp.bfloat16)
        tw_ref[rows, slots:2 * slots] = (re * s + im * c).astype(jnp.bfloat16)
    values = lax.dot_general(tw_ref[...], base_ref[0], (((1,), (1,)), ((), ())),
                             preferred_element_type=jnp.float32)
    lane = lax.broadcasted_iota(jnp.int32, (1, BLOCK), 1)
    for f in range(fields):
        for b in range(BLOCKS):
            v = values[depth * f + b:depth * f + b + 1, :]
            v = jnp.where(lane + BLOCK * b < points, v, 0.0)
            out_ref[0, f:f + 1, BLOCK * b:BLOCK * (b + 1)] = v.astype(jnp.bfloat16).astype(jnp.float32)


def synth(kernel, fourier, base_t, cos_t, sin_t, lengths, rowmap, fields, out_dtype, tw_rows):
    rows, cols, slots = fourier.shape
    depth = cos_t.shape[1]
    grid_spec = pltpu.PrefetchScalarGridSpec(
        num_scalar_prefetch=2,
        grid=(rows,),
        in_specs=[
            pl.BlockSpec((1, cols, slots), lambda r, n, m: (m[r], 0, 0)),
            pl.BlockSpec((1, BLOCK, 2 * slots), lambda r, n, m: (r, 0, 0)),
            pl.BlockSpec((1, depth, slots), lambda r, n, m: (r, 0, 0)),
            pl.BlockSpec((1, depth, slots), lambda r, n, m: (r, 0, 0)),
        ],
        out_specs=pl.BlockSpec((1, fields, LCAP), lambda r, n, m: (r, 0, 0)),
        scratch_shapes=[pltpu.VMEM((tw_rows, 2 * slots), jnp.bfloat16)],
    )
    return pl.pallas_call(
        kernel,
        grid_spec=grid_spec,
        out_shape=jax.ShapeDtypeStruct((rows, fields, LCAP), out_dtype),
        compiler_params=pltpu.CompilerParams(dimension_semantics=("arbitrary",)),
    )(lengths, rowmap, fourier, base_t, cos_t, sin_t)


def local(coefficients, legendre, pair_wave, row_points, layer_logpressure_factor):
    wave_count = lax.axis_size("wave")
    wave_rank = lax.axis_index("wave")
    pair_local, _, cols, pack_width = coefficients.shape
    fields = cols // 2
    half_rows = legendre.shape[3]
    all_rows = 2 * half_rows
    band_rows = all_rows // wave_count
    half_bands = half_rows // band_rows
    my_pairs = lax.dynamic_slice_in_dim(pair_wave, wave_rank * pair_local, pair_local)
    selection = pair_masks(my_pairs, pack_width).astype(jnp.bfloat16)
    coef = coefficients.reshape(pair_local, 2, fields, 2, pack_width).transpose(0, 1, 3, 2, 4)
    coef = coef.reshape(pair_local, 2, cols, pack_width)
    selected = coef[:, :, None, :, :] * selection[:, :, :, None, :]
    signs = jnp.array([[1.0, 1.0], [1.0, -1.0]], jnp.bfloat16)
    lhs = signs[None, :, :, None, None, None] * selected[:, None]
    sums = jnp.einsum("qaehci,qeit->qahct", lhs, legendre, preferred_element_type=jnp.float32)
    sums = sums.reshape(pair_local, 2, 2, cols, half_bands, band_rows)
    north = sums[:, 0]
    south = jnp.flip(sums[:, 1], 3)
    bands = jnp.concatenate([north, south], 3)
    send = bands.transpose(3, 0, 1, 4, 2).reshape(wave_count, pair_local * 2, band_rows * cols)
    got = lax.all_to_all(send, "wave", 0, 0, tiled=True)
    slots = got.shape[0] * got.shape[1]
    fourier = got.reshape(slots, band_rows * cols).T.reshape(band_rows, cols, slots)
    south_side = (wave_rank >= half_bands).astype(jnp.int32)
    local_rows = jnp.arange(band_rows, dtype=jnp.int32)
    rowmap = local_rows + south_side * (band_rows - 1 - 2 * local_rows)

    wave_numbers = jnp.stack([pair_wave, TRUNC - pair_wave], axis=1).reshape(-1)
    points_all = jnp.concatenate([row_points, jnp.flip(row_points)])
    lengths = lax.dynamic_slice_in_dim(points_all, wave_rank * band_rows, band_rows)
    base_t, cos_t, sin_t = tables(wave_numbers, lengths)
    heat_cols = fourier.reshape(band_rows, 2, fields // QUANTITY_COUNT, QUANTITY_COUNT, slots)[:, :, :, 0]
    heat_cols = heat_cols.reshape(band_rows, 2 * fields // QUANTITY_COUNT, slots)
    heat_fields = fields // QUANTITY_COUNT
    heat_state_values = synth(heat_kernel, heat_cols, base_t, cos_t, sin_t, lengths, rowmap,
                              heat_fields, jnp.float32, heat_fields * 48)
    values = synth(main_kernel, fourier, base_t, cos_t, sin_t, lengths, rowmap,
                   fields, jnp.bfloat16, fields * BLOCKS)

    device_layers = heat_state_values.shape[1]
    lev_rank = lax.axis_index("lev")
    layer_depth_factor = lax.dynamic_slice_in_dim(
        layer_logpressure_factor, lev_rank * device_layers, device_layers
    )
    scaled_heat_values = heat_state_values * layer_depth_factor[None, :, None]
    partial_totals = jnp.flip(jnp.cumsum(jnp.flip(scaled_heat_values, 1), axis=1), 1)
    everything = lax.all_gather(partial_totals[:, 0, :], "lev")
    lev_count = everything.shape[0]
    below = (jnp.arange(lev_count) > lev_rank).astype(jnp.float32)[:, None, None]
    deeper = jnp.sum(everything * below, axis=0)
    geopotential = (partial_totals + deeper[:, None, :]).astype(jnp.bfloat16)
    return (values, geopotential)


def solution(mesh):
    return jax.shard_map(
        local,
        mesh=mesh,
        in_specs=(P("wave", None, "lev", None), P("wave", None, None, None), P(), P(), P()),
        out_specs=(P("wave", "lev", None), P("wave", "lev", None)),
        check_vma=False,
    )
```

```python
import jax
import jax.numpy as jnp
from jax import lax
from jax.sharding import PartitionSpec as P
from jax.experimental import pallas as pl
from jax.experimental.pallas import tpu as pltpu

TRUNC = 1279
QUANTITY_COUNT = 4
LCAP = 5248
BLOCK = 128
BLOCKS = LCAP // BLOCK

two_pi = 6.283185307179586


def pair_masks(low_waves, pack_width):
    parity = jnp.arange(2, dtype=jnp.int32)
    low_count = (TRUNC - low_waves[:, None] - parity[None, :]) // 2 + 1
    high_count = (low_waves[:, None] - parity[None, :]) // 2 + 1
    pack_index = jnp.arange(pack_width, dtype=jnp.int32)[None, None, :]
    low_mask = pack_index < low_count[:, :, None]
    high_mask = (pack_index >= low_count[:, :, None]) & (
        pack_index < (low_count + high_count)[:, :, None]
    )
    return jnp.stack([low_mask, high_mask], axis=2)


def residue(j, points):
    q = jnp.floor(j.astype(jnp.float32) / points.astype(jnp.float32)).astype(jnp.int32)
    r = j - q * points
    r = jnp.where(r < 0, r + points, r)
    return jnp.where(r >= points, r - points, r)


def phase(waves, steps, points):
    j = waves * steps
    rem = residue(j, points)
    angle = rem.astype(jnp.float32) * (jnp.float32(two_pi) / points.astype(jnp.float32))
    return jnp.cos(angle), jnp.sin(angle)


def times(a, b):
    return a[0] * b[0] - a[1] * b[1], a[1] * b[0] + a[0] * b[1]


def tables(wave_numbers, lengths):
    rows = lengths.shape[0]
    slots = wave_numbers.shape[0]
    w = wave_numbers[None, None, :]
    pts = lengths[:, None, None]
    low = phase(w, jnp.arange(16, dtype=jnp.int32)[None, :, None], pts)
    high = phase(w, 16 * jnp.arange(8, dtype=jnp.int32)[None, :, None], pts)
    cos_b, sin_b = times(
        (high[0][:, :, None, :], high[1][:, :, None, :]),
        (low[0][:, None, :, :], low[1][:, None, :, :]),
    )
    base_t = jnp.concatenate(
        [cos_b.reshape(rows, BLOCK, slots), -sin_b.reshape(rows, BLOCK, slots)], axis=2
    ).astype(jnp.bfloat16)
    near = phase(w, BLOCK * jnp.arange(8, dtype=jnp.int32)[None, :, None], pts)
    far = phase(w, 8 * BLOCK * jnp.arange(6, dtype=jnp.int32)[None, :, None], pts)
    cos_t, sin_t = times(
        (far[0][:, :, None, :], far[1][:, :, None, :]),
        (near[0][:, None, :, :], near[1][:, None, :, :]),
    )
    wave_limit = jnp.minimum(TRUNC, (lengths - 1) // 2)
    keep = (wave_numbers[None, :] <= wave_limit[:, None]).astype(jnp.float32)[:, None, :]
    live = (jnp.arange(48) < BLOCKS).astype(jnp.float32)[None, :, None] * keep
    cos_t = cos_t.reshape(rows, 48, slots) * live
    sin_t = sin_t.reshape(rows, 48, slots) * live
    return base_t, cos_t, sin_t


def main_kernel(lengths_ref, rowmap_ref, f_ref, base_ref, cos_ref, sin_ref, out_ref, tw_ref):
    r = pl.program_id(0)
    points = lengths_ref[r]
    fields = out_ref.shape[1]
    slots = f_ref.shape[2]
    real_part = f_ref[0, 0:fields, :]
    imag_part = f_ref[0, fields:2 * fields, :]
    for b in range(BLOCKS):
        c = cos_ref[0, b:b + 1, :]
        s = sin_ref[0, b:b + 1, :]
        rows = slice(fields * b, fields * (b + 1))
        tw_ref[rows, 0:slots] = (real_part * c - imag_part * s).astype(jnp.bfloat16)
        tw_ref[rows, slots:2 * slots] = (real_part * s + imag_part * c).astype(jnp.bfloat16)
    values = lax.dot_general(tw_ref[...], base_ref[0], (((1,), (1,)), ((), ())),
                             preferred_element_type=jnp.float32)
    lane = lax.broadcasted_iota(jnp.int32, (fields, BLOCK), 1)
    for b in range(BLOCKS):
        v = values[fields * b:fields * (b + 1), :]
        v = jnp.where(lane + BLOCK * b < points, v, 0.0)
        out_ref[0, :, BLOCK * b:BLOCK * (b + 1)] = v.astype(jnp.bfloat16)


def heat_kernel(lengths_ref, rowmap_ref, f_ref, base_ref, cos_ref, sin_ref, out_ref, tw_ref):
    slots = f_ref.shape[2]
    depth = cos_ref.shape[1]
    fields = f_ref.shape[1] // 2
    c = cos_ref[0]
    s = sin_ref[0]
    for f in range(fields):
        re = f_ref[0, f:f + 1, :]
        im = f_ref[0, fields + f:fields + f + 1, :]
        rows = slice(depth * f, depth * (f + 1))
        tw_ref[rows, 0:slots] = (re * c - im * s).astype(jnp.bfloat16)
        tw_ref[rows, slots:2 * slots] = (re * s + im * c).astype(jnp.bfloat16)
    out_ref[0] = lax.dot_general(tw_ref[...], base_ref[0], (((1,), (1,)), ((), ())),
                                 preferred_element_type=jnp.float32)


def synth(kernel, fourier, base_t, cos_t, sin_t, lengths, rowmap, out_rows, out_cols, out_dtype, tw_rows):
    rows, cols, slots = fourier.shape
    depth = cos_t.shape[1]
    grid_spec = pltpu.PrefetchScalarGridSpec(
        num_scalar_prefetch=2,
        grid=(rows,),
        in_specs=[
            pl.BlockSpec((1, cols, slots), lambda r, n, m: (m[r], 0, 0)),
            pl.BlockSpec((1, BLOCK, 2 * slots), lambda r, n, m: (r, 0, 0)),
            pl.BlockSpec((1, depth, slots), lambda r, n, m: (r, 0, 0)),
            pl.BlockSpec((1, depth, slots), lambda r, n, m: (r, 0, 0)),
        ],
        out_specs=pl.BlockSpec((1, out_rows, out_cols), lambda r, n, m: (r, 0, 0)),
        scratch_shapes=[pltpu.VMEM((tw_rows, 2 * slots), jnp.bfloat16)],
    )
    return pl.pallas_call(
        kernel,
        grid_spec=grid_spec,
        out_shape=jax.ShapeDtypeStruct((rows, out_rows, out_cols), out_dtype),
        compiler_params=pltpu.CompilerParams(dimension_semantics=("arbitrary",)),
    )(lengths, rowmap, fourier, base_t, cos_t, sin_t)


def local(coefficients, legendre, pair_wave, row_points, layer_logpressure_factor):
    wave_count = lax.axis_size("wave")
    wave_rank = lax.axis_index("wave")
    pair_local, _, cols, pack_width = coefficients.shape
    fields = cols // 2
    half_rows = legendre.shape[3]
    all_rows = 2 * half_rows
    band_rows = all_rows // wave_count
    half_bands = half_rows // band_rows
    my_pairs = lax.dynamic_slice_in_dim(pair_wave, wave_rank * pair_local, pair_local)
    selection = pair_masks(my_pairs, pack_width).astype(jnp.bfloat16)
    coef = coefficients.reshape(pair_local, 2, fields, 2, pack_width).transpose(0, 1, 3, 2, 4)
    coef = coef.reshape(pair_local, 2, cols, pack_width)
    selected = coef[:, :, None, :, :] * selection[:, :, :, None, :]
    signs = jnp.array([[1.0, 1.0], [1.0, -1.0]], jnp.bfloat16)
    lhs = signs[None, :, :, None, None, None] * selected[:, None]
    sums = jnp.einsum("qaehci,qeit->qahct", lhs, legendre, preferred_element_type=jnp.float32)
    sums = sums.reshape(pair_local, 2, 2, cols, half_bands, band_rows)
    north = sums[:, 0]
    south = jnp.flip(sums[:, 1], 3)
    bands = jnp.concatenate([north, south], 3)
    send = bands.transpose(3, 0, 1, 2, 4).reshape(wave_count, pair_local * 2, cols * band_rows)
    got = lax.all_to_all(send.astype(jnp.bfloat16), "wave", 0, 0, tiled=True)
    slots = got.shape[0] * got.shape[1]
    fourier = got.reshape(slots, cols, band_rows).transpose(2, 1, 0).astype(jnp.float32)
    south_side = (wave_rank >= half_bands).astype(jnp.int32)
    local_rows = jnp.arange(band_rows, dtype=jnp.int32)
    rowmap = local_rows + south_side * (band_rows - 1 - 2 * local_rows)

    wave_numbers = jnp.stack([pair_wave, TRUNC - pair_wave], axis=1).reshape(-1)
    points_all = jnp.concatenate([row_points, jnp.flip(row_points)])
    lengths = lax.dynamic_slice_in_dim(points_all, wave_rank * band_rows, band_rows)
    base_t, cos_t, sin_t = tables(wave_numbers, lengths)
    heat_cols = fourier.reshape(band_rows, 2, fields // QUANTITY_COUNT, QUANTITY_COUNT, slots)[:, :, :, 0]
    heat_cols = heat_cols.reshape(band_rows, 2 * fields // QUANTITY_COUNT, slots)
    heat_fields = fields // QUANTITY_COUNT
    depth = cos_t.shape[1]
    raw = synth(heat_kernel, heat_cols, base_t, cos_t, sin_t, lengths, rowmap,
                heat_fields * depth, BLOCK, jnp.float32, heat_fields * depth)
    raw = raw.reshape(band_rows, heat_fields, depth, BLOCK)[:, :, :BLOCKS].reshape(band_rows, heat_fields, LCAP)
    position = jnp.arange(LCAP, dtype=jnp.int32)
    raw = jnp.where(position[None, None, :] < lengths[:, None, None], raw, 0.0)
    heat_state_values = raw.astype(jnp.bfloat16).astype(jnp.float32)
    values = synth(main_kernel, fourier, base_t, cos_t, sin_t, lengths, rowmap,
                   fields, LCAP, jnp.bfloat16, fields * BLOCKS)

    device_layers = heat_state_values.shape[1]
    lev_rank = lax.axis_index("lev")
    layer_depth_factor = lax.dynamic_slice_in_dim(
        layer_logpressure_factor, lev_rank * device_layers, device_layers
    )
    scaled_heat_values = heat_state_values * layer_depth_factor[None, :, None]
    partial_totals = jnp.flip(jnp.cumsum(jnp.flip(scaled_heat_values, 1), axis=1), 1)
    everything = lax.all_gather(partial_totals[:, 0, :], "lev")
    lev_count = everything.shape[0]
    below = (jnp.arange(lev_count) > lev_rank).astype(jnp.float32)[:, None, None]
    deeper = jnp.sum(everything * below, axis=0)
    geopotential = (partial_totals + deeper[:, None, :]).astype(jnp.bfloat16)
    return (values, geopotential)


def solution(mesh):
    return jax.shard_map(
        local,
        mesh=mesh,
        in_specs=(P("wave", None, "lev", None), P("wave", None, None, None), P(), P(), P()),
        out_specs=(P("wave", "lev", None), P("wave", "lev", None)),
        check_vma=False,
    )
```

```python
import jax
import jax.numpy as jnp
from jax import lax
from jax.sharding import PartitionSpec as P
from jax.experimental import pallas as pl
from jax.experimental.pallas import tpu as pltpu

TRUNC = 1279
QUANTITY_COUNT = 4
LCAP = 5248
BLOCK = 128
BLOCKS = LCAP // BLOCK
DEPTH = 48

two_pi = 6.283185307179586


def pair_masks(low_waves, pack_width):
    parity = jnp.arange(2, dtype=jnp.int32)
    low_count = (TRUNC - low_waves[:, None] - parity[None, :]) // 2 + 1
    high_count = (low_waves[:, None] - parity[None, :]) // 2 + 1
    pack_index = jnp.arange(pack_width, dtype=jnp.int32)[None, None, :]
    low_mask = pack_index < low_count[:, :, None]
    high_mask = (pack_index >= low_count[:, :, None]) & (
        pack_index < (low_count + high_count)[:, :, None]
    )
    return jnp.stack([low_mask, high_mask], axis=2)


def residue(j, points):
    q = jnp.floor(j.astype(jnp.float32) / points.astype(jnp.float32)).astype(jnp.int32)
    r = j - q * points
    r = jnp.where(r < 0, r + points, r)
    return jnp.where(r >= points, r - points, r)


def phase(waves, steps, points):
    j = waves * steps
    rem = residue(j, points)
    angle = rem.astype(jnp.float32) * (jnp.float32(two_pi) / points.astype(jnp.float32))
    return jnp.cos(angle), jnp.sin(angle)


def times(a, b):
    return a[0] * b[0] - a[1] * b[1], a[1] * b[0] + a[0] * b[1]


def tables(wave_numbers, lengths):
    w = wave_numbers[None, None, :]
    pts = lengths[:, None, None]
    low = phase(w, jnp.arange(16, dtype=jnp.int32)[None, :, None], pts)
    high = phase(w, 16 * jnp.arange(8, dtype=jnp.int32)[None, :, None], pts)
    near = phase(w, BLOCK * jnp.arange(8, dtype=jnp.int32)[None, :, None], pts)
    far = phase(w, 8 * BLOCK * jnp.arange(8, dtype=jnp.int32)[None, :, None], pts)
    wave_limit = jnp.minimum(TRUNC, (lengths - 1) // 2)
    keep = (wave_numbers[None, :] <= wave_limit[:, None]).astype(jnp.float32)[:, None, :]
    return jnp.concatenate(
        [low[0], low[1], high[0], high[1], near[0] * keep, near[1] * keep, far[0], far[1]], axis=1
    )


def expand(ph_ref, base_ref, tcos_ref, tsin_ref):
    slots = ph_ref.shape[2]
    p0c = ph_ref[0, 0:16, :]
    p0s = ph_ref[0, 16:32, :]
    for k1 in range(8):
        a = ph_ref[0, 32 + k1:33 + k1, :]
        b = ph_ref[0, 40 + k1:41 + k1, :]
        rows = slice(16 * k1, 16 * (k1 + 1))
        base_ref[rows, 0:slots] = (a * p0c - b * p0s).astype(jnp.bfloat16)
        base_ref[rows, slots:2 * slots] = (-(b * p0c + a * p0s)).astype(jnp.bfloat16)
    q0c = ph_ref[0, 48:56, :]
    q0s = ph_ref[0, 56:64, :]
    for b1 in range(6):
        a = ph_ref[0, 64 + b1:65 + b1, :]
        b = ph_ref[0, 72 + b1:73 + b1, :]
        rows = slice(8 * b1, 8 * (b1 + 1))
        tcos_ref[rows, :] = a * q0c - b * q0s
        tsin_ref[rows, :] = b * q0c + a * q0s


def main_kernel(lengths_ref, rowmap_ref, f_ref, ph_ref, out_ref, tw_ref, base_ref, cos_ref, sin_ref):
    expand(ph_ref, base_ref, cos_ref, sin_ref)
    r = pl.program_id(0)
    points = lengths_ref[r]
    fields = out_ref.shape[1]
    slots = f_ref.shape[2]
    real_part = f_ref[0, 0:fields, :]
    imag_part = f_ref[0, fields:2 * fields, :]
    for b in range(BLOCKS):
        c = cos_ref[b:b + 1, :]
        s = sin_ref[b:b + 1, :]
        rows = slice(fields * b, fields * (b + 1))
        tw_ref[rows, 0:slots] = (real_part * c - imag_part * s).astype(jnp.bfloat16)
        tw_ref[rows, slots:2 * slots] = (real_part * s + imag_part * c).astype(jnp.bfloat16)
    values = lax.dot_general(tw_ref[...], base_ref[...], (((1,), (1,)), ((), ())),
                             preferred_element_type=jnp.float32)
    lane = lax.broadcasted_iota(jnp.int32, (fields, BLOCK), 1)
    for b in range(BLOCKS):
        v = values[fields * b:fields * (b + 1), :]
        v = jnp.where(lane + BLOCK * b < points, v, 0.0)
        out_ref[0, :, BLOCK * b:BLOCK * (b + 1)] = v.astype(jnp.bfloat16)


def heat_kernel(lengths_ref, rowmap_ref, f_ref, ph_ref, out_ref, tw_ref, base_ref, cos_ref, sin_ref):
    expand(ph_ref, base_ref, cos_ref, sin_ref)
    slots = f_ref.shape[2]
    depth = cos_ref.shape[0]
    fields = f_ref.shape[1] // 2
    c = cos_ref[...]
    s = sin_ref[...]
    for f in range(fields):
        re = f_ref[0, f:f + 1, :]
        im = f_ref[0, fields + f:fields + f + 1, :]
        rows = slice(depth * f, depth * (f + 1))
        tw_ref[rows, 0:slots] = (re * c - im * s).astype(jnp.bfloat16)
        tw_ref[rows, slots:2 * slots] = (re * s + im * c).astype(jnp.bfloat16)
    out_ref[0] = lax.dot_general(tw_ref[...], base_ref[...], (((1,), (1,)), ((), ())),
                                 preferred_element_type=jnp.float32)


def synth(kernel, fourier, ph, lengths, rowmap, out_rows, out_cols, out_dtype, tw_rows):
    rows, cols, slots = fourier.shape
    grid_spec = pltpu.PrefetchScalarGridSpec(
        num_scalar_prefetch=2,
        grid=(rows,),
        in_specs=[
            pl.BlockSpec((1, cols, slots), lambda r, n, m: (m[r], 0, 0)),
            pl.BlockSpec((1, ph.shape[1], slots), lambda r, n, m: (r, 0, 0)),
        ],
        out_specs=pl.BlockSpec((1, out_rows, out_cols), lambda r, n, m: (r, 0, 0)),
        scratch_shapes=[
            pltpu.VMEM((tw_rows, 2 * slots), jnp.bfloat16),
            pltpu.VMEM((BLOCK, 2 * slots), jnp.bfloat16),
            pltpu.VMEM((DEPTH, slots), jnp.float32),
            pltpu.VMEM((DEPTH, slots), jnp.float32),
        ],
    )
    return pl.pallas_call(
        kernel,
        grid_spec=grid_spec,
        out_shape=jax.ShapeDtypeStruct((rows, out_rows, out_cols), out_dtype),
        compiler_params=pltpu.CompilerParams(dimension_semantics=("arbitrary",)),
    )(lengths, rowmap, fourier, ph)


def local(coefficients, legendre, pair_wave, row_points, layer_logpressure_factor):
    wave_count = lax.axis_size("wave")
    wave_rank = lax.axis_index("wave")
    pair_local, _, cols, pack_width = coefficients.shape
    fields = cols // 2
    half_rows = legendre.shape[3]
    all_rows = 2 * half_rows
    band_rows = all_rows // wave_count
    half_bands = half_rows // band_rows
    my_pairs = lax.dynamic_slice_in_dim(pair_wave, wave_rank * pair_local, pair_local)
    selection = pair_masks(my_pairs, pack_width).astype(jnp.bfloat16)
    coef = coefficients.reshape(pair_local, 2, fields, 2, pack_width).transpose(0, 1, 3, 2, 4)
    coef = coef.reshape(pair_local, 2, cols, pack_width)
    selected = coef[:, :, None, :, :] * selection[:, :, :, None, :]
    signs = jnp.array([[1.0, 1.0], [1.0, -1.0]], jnp.bfloat16)
    lhs = signs[None, :, :, None, None, None] * selected[:, None]
    sums = jnp.einsum("qaehci,qeit->qahct", lhs, legendre, preferred_element_type=jnp.float32)
    sums = sums.reshape(pair_local, 2, 2, cols, half_bands, band_rows)
    north = sums[:, 0]
    south = jnp.flip(sums[:, 1], 3)
    bands = jnp.concatenate([north, south], 3)
    send = bands.transpose(3, 0, 1, 4, 2).reshape(wave_count, pair_local * 2, band_rows * cols)
    got = lax.all_to_all(send, "wave", 0, 0, tiled=True)
    slots = got.shape[0] * got.shape[1]
    fourier = got.reshape(slots, band_rows * cols).T.reshape(band_rows, cols, slots)
    south_side = (wave_rank >= half_bands).astype(jnp.int32)
    local_rows = jnp.arange(band_rows, dtype=jnp.int32)
    rowmap = local_rows + south_side * (band_rows - 1 - 2 * local_rows)

    wave_numbers = jnp.stack([pair_wave, TRUNC - pair_wave], axis=1).reshape(-1)
    points_all = jnp.concatenate([row_points, jnp.flip(row_points)])
    lengths = lax.dynamic_slice_in_dim(points_all, wave_rank * band_rows, band_rows)
    ph = tables(wave_numbers, lengths)
    heat_cols = fourier.reshape(band_rows, 2, fields // QUANTITY_COUNT, QUANTITY_COUNT, slots)[:, :, :, 0]
    heat_cols = heat_cols.reshape(band_rows, 2 * fields // QUANTITY_COUNT, slots)
    heat_fields = fields // QUANTITY_COUNT
    depth = DEPTH
    raw = synth(heat_kernel, heat_cols, ph, lengths, rowmap,
                heat_fields * depth, BLOCK, jnp.float32, heat_fields * depth)
    raw = raw.reshape(band_rows, heat_fields, depth, BLOCK)[:, :, :BLOCKS].reshape(band_rows, heat_fields, LCAP)
    position = jnp.arange(LCAP, dtype=jnp.int32)
    raw = jnp.where(position[None, None, :] < lengths[:, None, None], raw, 0.0)
    heat_state_values = raw.astype(jnp.bfloat16).astype(jnp.float32)
    values = synth(main_kernel, fourier, ph, lengths, rowmap,
                   fields, LCAP, jnp.bfloat16, fields * BLOCKS)

    device_layers = heat_state_values.shape[1]
    lev_rank = lax.axis_index("lev")
    layer_depth_factor = lax.dynamic_slice_in_dim(
        layer_logpressure_factor, lev_rank * device_layers, device_layers
    )
    scaled_heat_values = heat_state_values * layer_depth_factor[None, :, None]
    partial_totals = jnp.flip(jnp.cumsum(jnp.flip(scaled_heat_values, 1), axis=1), 1)
    everything = lax.all_gather(partial_totals[:, 0, :], "lev")
    lev_count = everything.shape[0]
    below = (jnp.arange(lev_count) > lev_rank).astype(jnp.float32)[:, None, None]
    deeper = jnp.sum(everything * below, axis=0)
    geopotential = (partial_totals + deeper[:, None, :]).astype(jnp.bfloat16)
    return (values, geopotential)


def solution(mesh):
    return jax.shard_map(
        local,
        mesh=mesh,
        in_specs=(P("wave", None, "lev", None), P("wave", None, None, None), P(), P(), P()),
        out_specs=(P("wave", "lev", None), P("wave", "lev", None)),
        check_vma=False,
    )
```

```python
import jax
import jax.numpy as jnp
from jax import lax
from jax.sharding import PartitionSpec as P
from jax.experimental import pallas as pl
from jax.experimental.pallas import tpu as pltpu

TRUNC = 1279
QUANTITY_COUNT = 4
LCAP = 5248
BLOCK = 128
BLOCKS = LCAP // BLOCK
DEPTH = 48

two_pi = 6.283185307179586


def pair_masks(low_waves, pack_width):
    parity = jnp.arange(2, dtype=jnp.int32)
    low_count = (TRUNC - low_waves[:, None] - parity[None, :]) // 2 + 1
    high_count = (low_waves[:, None] - parity[None, :]) // 2 + 1
    pack_index = jnp.arange(pack_width, dtype=jnp.int32)[None, None, :]
    low_mask = pack_index < low_count[:, :, None]
    high_mask = (pack_index >= low_count[:, :, None]) & (
        pack_index < (low_count + high_count)[:, :, None]
    )
    return jnp.stack([low_mask, high_mask], axis=2)


def residue(j, points):
    q = jnp.floor(j.astype(jnp.float32) / points.astype(jnp.float32)).astype(jnp.int32)
    r = j - q * points
    r = jnp.where(r < 0, r + points, r)
    return jnp.where(r >= points, r - points, r)


def phase(waves, steps, points):
    j = waves * steps
    rem = residue(j, points)
    angle = rem.astype(jnp.float32) * (jnp.float32(two_pi) / points.astype(jnp.float32))
    return jnp.cos(angle), jnp.sin(angle)


def times(a, b):
    return a[0] * b[0] - a[1] * b[1], a[1] * b[0] + a[0] * b[1]


def tables(wave_numbers, lengths):
    w = wave_numbers[None, None, :]
    pts = lengths[:, None, None]
    low = phase(w, jnp.arange(16, dtype=jnp.int32)[None, :, None], pts)
    high = phase(w, 16 * jnp.arange(8, dtype=jnp.int32)[None, :, None], pts)
    near = phase(w, BLOCK * jnp.arange(8, dtype=jnp.int32)[None, :, None], pts)
    far = phase(w, 8 * BLOCK * jnp.arange(8, dtype=jnp.int32)[None, :, None], pts)
    wave_limit = jnp.minimum(TRUNC, (lengths - 1) // 2)
    keep = (wave_numbers[None, :] <= wave_limit[:, None]).astype(jnp.float32)[:, None, :]
    return jnp.concatenate(
        [low[0], low[1], high[0], high[1], near[0] * keep, near[1] * keep, far[0], far[1]], axis=1
    )


def expand(ph_ref, base_ref, tcos_ref, tsin_ref):
    slots = ph_ref.shape[2]
    p0c = ph_ref[0, 0:16, :]
    p0s = ph_ref[0, 16:32, :]
    for k1 in range(8):
        a = ph_ref[0, 32 + k1:33 + k1, :]
        b = ph_ref[0, 40 + k1:41 + k1, :]
        rows = slice(16 * k1, 16 * (k1 + 1))
        base_ref[rows, 0:slots] = (a * p0c - b * p0s).astype(jnp.bfloat16)
        base_ref[rows, slots:2 * slots] = (-(b * p0c + a * p0s)).astype(jnp.bfloat16)
    q0c = ph_ref[0, 48:56, :]
    q0s = ph_ref[0, 56:64, :]
    for b1 in range(6):
        a = ph_ref[0, 64 + b1:65 + b1, :]
        b = ph_ref[0, 72 + b1:73 + b1, :]
        rows = slice(8 * b1, 8 * (b1 + 1))
        tcos_ref[rows, :] = a * q0c - b * q0s
        tsin_ref[rows, :] = b * q0c + a * q0s


def main_kernel(lengths_ref, rowmap_ref, f_ref, ph_ref, out_ref, tw_ref, base_ref, cos_ref, sin_ref):
    expand(ph_ref, base_ref, cos_ref, sin_ref)
    r = pl.program_id(0)
    points = lengths_ref[r]
    fields = out_ref.shape[1]
    slots = f_ref.shape[2]
    real_part = f_ref[0, 0:fields, :]
    imag_part = f_ref[0, fields:2 * fields, :]
    for b in range(BLOCKS):
        c = cos_ref[b:b + 1, :]
        s = sin_ref[b:b + 1, :]
        rows = slice(fields * b, fields * (b + 1))
        tw_ref[rows, 0:slots] = (real_part * c - imag_part * s).astype(jnp.bfloat16)
        tw_ref[rows, slots:2 * slots] = (real_part * s + imag_part * c).astype(jnp.bfloat16)
    values = lax.dot_general(tw_ref[...], base_ref[...], (((1,), (1,)), ((), ())),
                             preferred_element_type=jnp.float32)
    lane = lax.broadcasted_iota(jnp.int32, (fields, BLOCK), 1)
    for b in range(BLOCKS):
        v = values[fields * b:fields * (b + 1), :]
        v = jnp.where(lane + BLOCK * b < points, v, 0.0)
        out_ref[0, :, BLOCK * b:BLOCK * (b + 1)] = v.astype(jnp.bfloat16)


def heat_kernel(lengths_ref, rowmap_ref, f_ref, ph_ref, out_ref, tw_ref, base_ref, cos_ref, sin_ref):
    expand(ph_ref, base_ref, cos_ref, sin_ref)
    slots = f_ref.shape[2]
    depth = cos_ref.shape[0]
    fields = f_ref.shape[1] // 2
    c = cos_ref[...]
    s = sin_ref[...]
    for f in range(fields):
        re = f_ref[0, f:f + 1, :]
        im = f_ref[0, fields + f:fields + f + 1, :]
        rows = slice(depth * f, depth * (f + 1))
        tw_ref[rows, 0:slots] = (re * c - im * s).astype(jnp.bfloat16)
        tw_ref[rows, slots:2 * slots] = (re * s + im * c).astype(jnp.bfloat16)
    out_ref[0] = lax.dot_general(tw_ref[...], base_ref[...], (((1,), (1,)), ((), ())),
                                 preferred_element_type=jnp.float32)


def synth(kernel, fourier, ph, lengths, rowmap, out_rows, out_cols, out_dtype, tw_rows):
    rows, cols, slots = fourier.shape
    grid_spec = pltpu.PrefetchScalarGridSpec(
        num_scalar_prefetch=2,
        grid=(rows,),
        in_specs=[
            pl.BlockSpec((1, cols, slots), lambda r, n, m: (m[r], 0, 0)),
            pl.BlockSpec((1, ph.shape[1], slots), lambda r, n, m: (r, 0, 0)),
        ],
        out_specs=pl.BlockSpec((1, out_rows, out_cols), lambda r, n, m: (r, 0, 0)),
        scratch_shapes=[
            pltpu.VMEM((tw_rows, 2 * slots), jnp.bfloat16),
            pltpu.VMEM((BLOCK, 2 * slots), jnp.bfloat16),
            pltpu.VMEM((DEPTH, slots), jnp.float32),
            pltpu.VMEM((DEPTH, slots), jnp.float32),
        ],
    )
    return pl.pallas_call(
        kernel,
        grid_spec=grid_spec,
        out_shape=jax.ShapeDtypeStruct((rows, out_rows, out_cols), out_dtype),
        compiler_params=pltpu.CompilerParams(dimension_semantics=("arbitrary",)),
    )(lengths, rowmap, fourier, ph)


def local(coefficients, legendre, pair_wave, row_points, layer_logpressure_factor):
    wave_count = lax.axis_size("wave")
    wave_rank = lax.axis_index("wave")
    pair_local, _, cols, pack_width = coefficients.shape
    fields = cols // 2
    half_rows = legendre.shape[3]
    all_rows = 2 * half_rows
    band_rows = all_rows // wave_count
    half_bands = half_rows // band_rows
    my_pairs = lax.dynamic_slice_in_dim(pair_wave, wave_rank * pair_local, pair_local)
    selection = pair_masks(my_pairs, pack_width).astype(jnp.bfloat16)
    coef = coefficients.reshape(pair_local, 2, fields, 2, pack_width).transpose(0, 1, 3, 2, 4)
    coef = coef.reshape(pair_local, 2, cols, pack_width)
    selected = coef[:, :, None, :, :] * selection[:, :, :, None, :]
    signs = jnp.array([[1.0, 1.0], [1.0, -1.0]], jnp.bfloat16)
    lhs = signs[None, :, :, None, None, None] * selected[:, None]
    chunks = 2
    part = pair_local // chunks
    pieces = []
    for k in range(chunks):
        pick = slice(part * k, part * (k + 1))
        sums = jnp.einsum("qaehci,qeit->qahct", lhs[pick], legendre[pick],
                          preferred_element_type=jnp.float32)
        sums = sums.reshape(part, 2, 2, cols, half_bands, band_rows)
        north = sums[:, 0]
        south = jnp.flip(sums[:, 1], 3)
        bands = jnp.concatenate([north, south], 3)
        send = bands.transpose(3, 0, 1, 4, 2).reshape(wave_count, part * 2, band_rows * cols)
        pieces.append(lax.all_to_all(send, "wave", 0, 0, tiled=True))
    got = jnp.concatenate(pieces, axis=1)
    slots = got.shape[0] * got.shape[1]
    fourier = got.reshape(slots, band_rows * cols).T.reshape(band_rows, cols, slots)
    south_side = (wave_rank >= half_bands).astype(jnp.int32)
    local_rows = jnp.arange(band_rows, dtype=jnp.int32)
    rowmap = local_rows + south_side * (band_rows - 1 - 2 * local_rows)

    wave_numbers = jnp.stack([pair_wave, TRUNC - pair_wave], axis=1).reshape(-1)
    points_all = jnp.concatenate([row_points, jnp.flip(row_points)])
    lengths = lax.dynamic_slice_in_dim(points_all, wave_rank * band_rows, band_rows)
    ph = tables(wave_numbers, lengths)
    heat_cols = fourier.reshape(band_rows, 2, fields // QUANTITY_COUNT, QUANTITY_COUNT, slots)[:, :, :, 0]
    heat_cols = heat_cols.reshape(band_rows, 2 * fields // QUANTITY_COUNT, slots)
    heat_fields = fields // QUANTITY_COUNT
    depth = DEPTH
    raw = synth(heat_kernel, heat_cols, ph, lengths, rowmap,
                heat_fields * depth, BLOCK, jnp.float32, heat_fields * depth)
    raw = raw.reshape(band_rows, heat_fields, depth, BLOCK)[:, :, :BLOCKS].reshape(band_rows, heat_fields, LCAP)
    position = jnp.arange(LCAP, dtype=jnp.int32)
    raw = jnp.where(position[None, None, :] < lengths[:, None, None], raw, 0.0)
    heat_state_values = raw.astype(jnp.bfloat16).astype(jnp.float32)
    values = synth(main_kernel, fourier, ph, lengths, rowmap,
                   fields, LCAP, jnp.bfloat16, fields * BLOCKS)

    device_layers = heat_state_values.shape[1]
    lev_rank = lax.axis_index("lev")
    layer_depth_factor = lax.dynamic_slice_in_dim(
        layer_logpressure_factor, lev_rank * device_layers, device_layers
    )
    scaled_heat_values = heat_state_values * layer_depth_factor[None, :, None]
    partial_totals = jnp.flip(jnp.cumsum(jnp.flip(scaled_heat_values, 1), axis=1), 1)
    everything = lax.all_gather(partial_totals[:, 0, :], "lev")
    lev_count = everything.shape[0]
    below = (jnp.arange(lev_count) > lev_rank).astype(jnp.float32)[:, None, None]
    deeper = jnp.sum(everything * below, axis=0)
    geopotential = (partial_totals + deeper[:, None, :]).astype(jnp.bfloat16)
    return (values, geopotential)


def solution(mesh):
    return jax.shard_map(
        local,
        mesh=mesh,
        in_specs=(P("wave", None, "lev", None), P("wave", None, None, None), P(), P(), P()),
        out_specs=(P("wave", "lev", None), P("wave", "lev", None)),
        check_vma=False,
    )
```

```python
import jax
import jax.numpy as jnp
from jax import lax
from jax.sharding import PartitionSpec as P
from jax.experimental import pallas as pl
from jax.experimental.pallas import tpu as pltpu

TRUNC = 1279
QUANTITY_COUNT = 4
LCAP = 5248
BLOCK = 128
BLOCKS = LCAP // BLOCK
DEPTH = 48

two_pi = 6.283185307179586


def pair_masks(low_waves, pack_width):
    parity = jnp.arange(2, dtype=jnp.int32)
    low_count = (TRUNC - low_waves[:, None] - parity[None, :]) // 2 + 1
    high_count = (low_waves[:, None] - parity[None, :]) // 2 + 1
    pack_index = jnp.arange(pack_width, dtype=jnp.int32)[None, None, :]
    low_mask = pack_index < low_count[:, :, None]
    high_mask = (pack_index >= low_count[:, :, None]) & (
        pack_index < (low_count + high_count)[:, :, None]
    )
    return jnp.stack([low_mask, high_mask], axis=2)


def residue(j, points):
    q = jnp.floor(j.astype(jnp.float32) / points.astype(jnp.float32)).astype(jnp.int32)
    r = j - q * points
    r = jnp.where(r < 0, r + points, r)
    return jnp.where(r >= points, r - points, r)


def phase(waves, steps, points):
    j = waves * steps
    rem = residue(j, points)
    angle = rem.astype(jnp.float32) * (jnp.float32(two_pi) / points.astype(jnp.float32))
    return jnp.cos(angle), jnp.sin(angle)


def times(a, b):
    return a[0] * b[0] - a[1] * b[1], a[1] * b[0] + a[0] * b[1]


def tables(wave_numbers, lengths):
    w = wave_numbers[None, None, :]
    pts = lengths[:, None, None]
    low = phase(w, jnp.arange(16, dtype=jnp.int32)[None, :, None], pts)
    high = phase(w, 16 * jnp.arange(8, dtype=jnp.int32)[None, :, None], pts)
    near = phase(w, BLOCK * jnp.arange(8, dtype=jnp.int32)[None, :, None], pts)
    far = phase(w, 8 * BLOCK * jnp.arange(8, dtype=jnp.int32)[None, :, None], pts)
    wave_limit = jnp.minimum(TRUNC, (lengths - 1) // 2)
    keep = (wave_numbers[None, :] <= wave_limit[:, None]).astype(jnp.float32)[:, None, :]
    return jnp.concatenate(
        [low[0], low[1], high[0], high[1], near[0] * keep, near[1] * keep, far[0], far[1]], axis=1
    )


def expand(ph_ref, base_ref, tcos_ref, tsin_ref):
    slots = ph_ref.shape[2]
    p0c = ph_ref[0, 0:16, :]
    p0s = ph_ref[0, 16:32, :]
    for k1 in range(8):
        a = ph_ref[0, 32 + k1:33 + k1, :]
        b = ph_ref[0, 40 + k1:41 + k1, :]
        rows = slice(16 * k1, 16 * (k1 + 1))
        base_ref[rows, 0:slots] = (a * p0c - b * p0s).astype(jnp.bfloat16)
        base_ref[rows, slots:2 * slots] = (-(b * p0c + a * p0s)).astype(jnp.bfloat16)
    q0c = ph_ref[0, 48:56, :]
    q0s = ph_ref[0, 56:64, :]
    for b1 in range(6):
        a = ph_ref[0, 64 + b1:65 + b1, :]
        b = ph_ref[0, 72 + b1:73 + b1, :]
        rows = slice(8 * b1, 8 * (b1 + 1))
        tcos_ref[rows, :] = a * q0c - b * q0s
        tsin_ref[rows, :] = b * q0c + a * q0s


def main_kernel(lengths_ref, rowmap_ref, f_ref, ph_ref, out_ref, tw_ref, base_ref, cos_ref, sin_ref):
    expand(ph_ref, base_ref, cos_ref, sin_ref)
    r = pl.program_id(0)
    points = lengths_ref[r]
    fields = out_ref.shape[1]
    slots = f_ref.shape[2]
    real_part = f_ref[0, 0:fields, :]
    imag_part = f_ref[0, fields:2 * fields, :]
    for b in range(BLOCKS):
        c = cos_ref[b:b + 1, :]
        s = sin_ref[b:b + 1, :]
        rows = slice(fields * b, fields * (b + 1))
        tw_ref[rows, 0:slots] = (real_part * c - imag_part * s).astype(jnp.bfloat16)
        tw_ref[rows, slots:2 * slots] = (real_part * s + imag_part * c).astype(jnp.bfloat16)
    values = lax.dot_general(tw_ref[...], base_ref[...], (((1,), (1,)), ((), ())),
                             preferred_element_type=jnp.float32)
    lane = lax.broadcasted_iota(jnp.int32, (fields, BLOCK), 1)
    for b in range(BLOCKS):
        v = values[fields * b:fields * (b + 1), :]
        v = jnp.where(lane + BLOCK * b < points, v, 0.0)
        out_ref[0, :, BLOCK * b:BLOCK * (b + 1)] = v.astype(jnp.bfloat16)


def heat_kernel(lengths_ref, rowmap_ref, f_ref, ph_ref, out_ref, tw_ref, base_ref, cos_ref, sin_ref):
    expand(ph_ref, base_ref, cos_ref, sin_ref)
    slots = f_ref.shape[2]
    depth = cos_ref.shape[0]
    fields = f_ref.shape[1] // 2
    c = cos_ref[...]
    s = sin_ref[...]
    for f in range(fields):
        re = f_ref[0, f:f + 1, :]
        im = f_ref[0, fields + f:fields + f + 1, :]
        rows = slice(depth * f, depth * (f + 1))
        tw_ref[rows, 0:slots] = (re * c - im * s).astype(jnp.bfloat16)
        tw_ref[rows, slots:2 * slots] = (re * s + im * c).astype(jnp.bfloat16)
    out_ref[0] = lax.dot_general(tw_ref[...], base_ref[...], (((1,), (1,)), ((), ())),
                                 preferred_element_type=jnp.float32)


def synth(kernel, fourier, ph, lengths, rowmap, out_rows, out_cols, out_dtype, tw_rows):
    rows, cols, slots = fourier.shape
    grid_spec = pltpu.PrefetchScalarGridSpec(
        num_scalar_prefetch=2,
        grid=(rows,),
        in_specs=[
            pl.BlockSpec((1, cols, slots), lambda r, n, m: (m[r], 0, 0)),
            pl.BlockSpec((1, ph.shape[1], slots), lambda r, n, m: (r, 0, 0)),
        ],
        out_specs=pl.BlockSpec((1, out_rows, out_cols), lambda r, n, m: (r, 0, 0)),
        scratch_shapes=[
            pltpu.VMEM((tw_rows, 2 * slots), jnp.bfloat16),
            pltpu.VMEM((BLOCK, 2 * slots), jnp.bfloat16),
            pltpu.VMEM((DEPTH, slots), jnp.float32),
            pltpu.VMEM((DEPTH, slots), jnp.float32),
        ],
    )
    return pl.pallas_call(
        kernel,
        grid_spec=grid_spec,
        out_shape=jax.ShapeDtypeStruct((rows, out_rows, out_cols), out_dtype),
        compiler_params=pltpu.CompilerParams(dimension_semantics=("arbitrary",)),
    )(lengths, rowmap, fourier, ph)


def local(coefficients, legendre, pair_wave, row_points, layer_logpressure_factor):
    wave_count = lax.axis_size("wave")
    wave_rank = lax.axis_index("wave")
    pair_local, _, cols, pack_width = coefficients.shape
    fields = cols // 2
    half_rows = legendre.shape[3]
    all_rows = 2 * half_rows
    band_rows = all_rows // wave_count
    half_bands = half_rows // band_rows
    my_pairs = lax.dynamic_slice_in_dim(pair_wave, wave_rank * pair_local, pair_local)
    selection = pair_masks(my_pairs, pack_width).astype(jnp.bfloat16)
    coef = coefficients.reshape(pair_local, 2, fields, 2, pack_width).transpose(0, 1, 3, 2, 4)
    coef = coef.reshape(pair_local, 2, cols, pack_width)
    selected = coef[:, :, None, :, :] * selection[:, :, :, None, :]
    signs = jnp.array([[1.0, 1.0], [1.0, -1.0]], jnp.bfloat16)
    lhs = signs[None, :, :, None, None, None] * selected[:, None]
    sums = jnp.einsum("qaehci,qeit->qahct", lhs, legendre, preferred_element_type=jnp.float32)
    sums = sums.reshape(pair_local, 2, 2, cols, half_bands, band_rows)
    north = sums[:, 0]
    south = jnp.flip(sums[:, 1], 3)
    bands = jnp.concatenate([north, south], 3)
    send = bands.transpose(3, 0, 1, 4, 2).reshape(wave_count, pair_local * 2, band_rows * cols)
    got = lax.all_to_all(send, "wave", 0, 0, tiled=True)
    slots = got.shape[0] * got.shape[1]
    fourier = got.reshape(slots, band_rows * cols).T.reshape(band_rows, cols, slots)
    south_side = (wave_rank >= half_bands).astype(jnp.int32)
    local_rows = jnp.arange(band_rows, dtype=jnp.int32)
    rowmap = local_rows + south_side * (band_rows - 1 - 2 * local_rows)

    wave_numbers = jnp.stack([pair_wave, TRUNC - pair_wave], axis=1).reshape(-1)
    points_all = jnp.concatenate([row_points, jnp.flip(row_points)])
    lengths = lax.dynamic_slice_in_dim(points_all, wave_rank * band_rows, band_rows)
    ph = tables(wave_numbers, lengths)
    values = synth(main_kernel, fourier, ph, lengths, rowmap,
                   fields, LCAP, jnp.bfloat16, fields * BLOCKS)
    heat_state_values = values[:, 0::QUANTITY_COUNT, :].astype(jnp.float32)

    device_layers = heat_state_values.shape[1]
    lev_rank = lax.axis_index("lev")
    layer_depth_factor = lax.dynamic_slice_in_dim(
        layer_logpressure_factor, lev_rank * device_layers, device_layers
    )
    scaled_heat_values = heat_state_values * layer_depth_factor[None, :, None]
    partial_totals = jnp.flip(jnp.cumsum(jnp.flip(scaled_heat_values, 1), axis=1), 1)
    lev_count = lax.axis_size("lev")
    bottom = partial_totals[:, 0, :]
    next_one = lax.ppermute(bottom, "lev", [(d + 1, d) for d in range(lev_count - 1)])
    pair_sum = bottom + next_one
    next_two = lax.ppermute(pair_sum, "lev", [(d + 2, d) for d in range(lev_count - 2)])
    deeper = next_one + next_two
    geopotential = (partial_totals + deeper[:, None, :]).astype(jnp.bfloat16)
    return (values, geopotential)


def solution(mesh):
    return jax.shard_map(
        local,
        mesh=mesh,
        in_specs=(P("wave", None, "lev", None), P("wave", None, None, None), P(), P(), P()),
        out_specs=(P("wave", "lev", None), P("wave", "lev", None)),
        check_vma=False,
    )
```

```python
import jax
import jax.numpy as jnp
from jax import lax
from jax.sharding import PartitionSpec as P
from jax.experimental import pallas as pl
from jax.experimental.pallas import tpu as pltpu

TRUNC = 1279
QUANTITY_COUNT = 4
LCAP = 5248
BLOCK = 128
BLOCKS = LCAP // BLOCK
DEPTH = 48

two_pi = 6.283185307179586


def pair_masks(low_waves, pack_width):
    parity = jnp.arange(2, dtype=jnp.int32)
    low_count = (TRUNC - low_waves[:, None] - parity[None, :]) // 2 + 1
    high_count = (low_waves[:, None] - parity[None, :]) // 2 + 1
    pack_index = jnp.arange(pack_width, dtype=jnp.int32)[None, None, :]
    low_mask = pack_index < low_count[:, :, None]
    high_mask = (pack_index >= low_count[:, :, None]) & (
        pack_index < (low_count + high_count)[:, :, None]
    )
    return jnp.stack([low_mask, high_mask], axis=2)


def residue(j, points):
    q = jnp.floor(j.astype(jnp.float32) / points.astype(jnp.float32)).astype(jnp.int32)
    r = j - q * points
    r = jnp.where(r < 0, r + points, r)
    return jnp.where(r >= points, r - points, r)


def phase(waves, steps, points):
    j = waves * steps
    rem = residue(j, points)
    angle = rem.astype(jnp.float32) * (jnp.float32(two_pi) / points.astype(jnp.float32))
    return jnp.cos(angle), jnp.sin(angle)


def times(a, b):
    return a[0] * b[0] - a[1] * b[1], a[1] * b[0] + a[0] * b[1]


def tables(wave_numbers, lengths):
    w = wave_numbers[None, None, :]
    pts = lengths[:, None, None]
    low = phase(w, jnp.arange(16, dtype=jnp.int32)[None, :, None], pts)
    high = phase(w, 16 * jnp.arange(8, dtype=jnp.int32)[None, :, None], pts)
    near = phase(w, BLOCK * jnp.arange(8, dtype=jnp.int32)[None, :, None], pts)
    far = phase(w, 8 * BLOCK * jnp.arange(8, dtype=jnp.int32)[None, :, None], pts)
    wave_limit = jnp.minimum(TRUNC, (lengths - 1) // 2)
    keep = (wave_numbers[None, :] <= wave_limit[:, None]).astype(jnp.float32)[:, None, :]
    return jnp.concatenate(
        [low[0], low[1], high[0], high[1], near[0] * keep, near[1] * keep, far[0], far[1]], axis=1
    )


def expand(ph_ref, base_ref, tcos_ref, tsin_ref):
    slots = ph_ref.shape[2]
    p0c = ph_ref[0, 0:16, :]
    p0s = ph_ref[0, 16:32, :]
    for k1 in range(8):
        a = ph_ref[0, 32 + k1:33 + k1, :]
        b = ph_ref[0, 40 + k1:41 + k1, :]
        rows = slice(16 * k1, 16 * (k1 + 1))
        base_ref[rows, 0:slots] = (a * p0c - b * p0s).astype(jnp.bfloat16)
        base_ref[rows, slots:2 * slots] = (-(b * p0c + a * p0s)).astype(jnp.bfloat16)
    q0c = ph_ref[0, 48:56, :]
    q0s = ph_ref[0, 56:64, :]
    for b1 in range(6):
        a = ph_ref[0, 64 + b1:65 + b1, :]
        b = ph_ref[0, 72 + b1:73 + b1, :]
        rows = slice(8 * b1, 8 * (b1 + 1))
        tcos_ref[rows, :] = a * q0c - b * q0s
        tsin_ref[rows, :] = b * q0c + a * q0s


def main_kernel(lengths_ref, rowmap_ref, f_ref, ph_ref, out_ref, heat_ref, tw_ref, base_ref, cos_ref,
                sin_ref, kept_ref):
    expand(ph_ref, base_ref, cos_ref, sin_ref)
    r = pl.program_id(0)
    points = lengths_ref[r]
    fields = out_ref.shape[1]
    slots = f_ref.shape[2]
    real_part = f_ref[0, 0:fields, :]
    imag_part = f_ref[0, fields:2 * fields, :]
    for b in range(BLOCKS):
        c = cos_ref[b:b + 1, :]
        s = sin_ref[b:b + 1, :]
        rows = slice(fields * b, fields * (b + 1))
        tw_ref[rows, 0:slots] = (real_part * c - imag_part * s).astype(jnp.bfloat16)
        tw_ref[rows, slots:2 * slots] = (real_part * s + imag_part * c).astype(jnp.bfloat16)
    values = lax.dot_general(tw_ref[...], base_ref[...], (((1,), (1,)), ((), ())),
                             preferred_element_type=jnp.float32)
    lane = lax.broadcasted_iota(jnp.int32, (fields, BLOCK), 1)
    for b in range(BLOCKS):
        v = values[fields * b:fields * (b + 1), :]
        v = jnp.where(lane + BLOCK * b < points, v, 0.0).astype(jnp.bfloat16)
        out_ref[0, :, BLOCK * b:BLOCK * (b + 1)] = v
        kept_ref[fields * b:fields * (b + 1), :] = v.astype(jnp.float32)
    levels = heat_ref.shape[1]
    for level in range(levels):
        heat_ref[0, level] = kept_ref[pl.ds(QUANTITY_COUNT * level, BLOCKS, stride=fields), :]


def synth(fourier, ph, lengths, rowmap):
    rows, cols, slots = fourier.shape
    fields = cols // 2
    levels = fields // QUANTITY_COUNT
    grid_spec = pltpu.PrefetchScalarGridSpec(
        num_scalar_prefetch=2,
        grid=(rows,),
        in_specs=[
            pl.BlockSpec((1, cols, slots), lambda r, n, m: (m[r], 0, 0)),
            pl.BlockSpec((1, ph.shape[1], slots), lambda r, n, m: (r, 0, 0)),
        ],
        out_specs=[
            pl.BlockSpec((1, fields, LCAP), lambda r, n, m: (r, 0, 0)),
            pl.BlockSpec((1, levels, BLOCKS, BLOCK), lambda r, n, m: (r, 0, 0, 0)),
        ],
        scratch_shapes=[
            pltpu.VMEM((fields * BLOCKS, 2 * slots), jnp.bfloat16),
            pltpu.VMEM((BLOCK, 2 * slots), jnp.bfloat16),
            pltpu.VMEM((DEPTH, slots), jnp.float32),
            pltpu.VMEM((DEPTH, slots), jnp.float32),
            pltpu.VMEM((fields * BLOCKS, BLOCK), jnp.float32),
        ],
    )
    return pl.pallas_call(
        main_kernel,
        grid_spec=grid_spec,
        out_shape=(
            jax.ShapeDtypeStruct((rows, fields, LCAP), jnp.bfloat16),
            jax.ShapeDtypeStruct((rows, levels, BLOCKS, BLOCK), jnp.float32),
        ),
        compiler_params=pltpu.CompilerParams(dimension_semantics=("arbitrary",)),
    )(lengths, rowmap, fourier, ph)


def local(coefficients, legendre, pair_wave, row_points, layer_logpressure_factor):
    wave_count = lax.axis_size("wave")
    wave_rank = lax.axis_index("wave")
    pair_local, _, cols, pack_width = coefficients.shape
    fields = cols // 2
    half_rows = legendre.shape[3]
    all_rows = 2 * half_rows
    band_rows = all_rows // wave_count
    half_bands = half_rows // band_rows
    my_pairs = lax.dynamic_slice_in_dim(pair_wave, wave_rank * pair_local, pair_local)
    selection = pair_masks(my_pairs, pack_width).astype(jnp.bfloat16)
    coef = coefficients.reshape(pair_local, 2, fields, 2, pack_width).transpose(0, 1, 3, 2, 4)
    coef = coef.reshape(pair_local, 2, cols, pack_width)
    selected = coef[:, :, None, :, :] * selection[:, :, :, None, :]
    signs = jnp.array([[1.0, 1.0], [1.0, -1.0]], jnp.bfloat16)
    lhs = signs[None, :, :, None, None, None] * selected[:, None]
    sums = jnp.einsum("qaehci,qeit->qahct", lhs, legendre, preferred_element_type=jnp.float32)
    sums = sums.reshape(pair_local, 2, 2, cols, half_bands, band_rows)
    north = sums[:, 0]
    south = jnp.flip(sums[:, 1], 3)
    bands = jnp.concatenate([north, south], 3)
    send = bands.transpose(3, 0, 1, 4, 2).reshape(wave_count, pair_local * 2, band_rows * cols)
    got = lax.all_to_all(send, "wave", 0, 0, tiled=True)
    slots = got.shape[0] * got.shape[1]
    fourier = got.reshape(slots, band_rows * cols).T.reshape(band_rows, cols, slots)
    south_side = (wave_rank >= half_bands).astype(jnp.int32)
    local_rows = jnp.arange(band_rows, dtype=jnp.int32)
    rowmap = local_rows + south_side * (band_rows - 1 - 2 * local_rows)

    wave_numbers = jnp.stack([pair_wave, TRUNC - pair_wave], axis=1).reshape(-1)
    points_all = jnp.concatenate([row_points, jnp.flip(row_points)])
    lengths = lax.dynamic_slice_in_dim(points_all, wave_rank * band_rows, band_rows)
    ph = tables(wave_numbers, lengths)
    values, heat = synth(fourier, ph, lengths, rowmap)
    heat_state_values = heat.reshape(band_rows, fields // QUANTITY_COUNT, LCAP)

    device_layers = heat_state_values.shape[1]
    lev_rank = lax.axis_index("lev")
    layer_depth_factor = lax.dynamic_slice_in_dim(
        layer_logpressure_factor, lev_rank * device_layers, device_layers
    )
    scaled_heat_values = heat_state_values * layer_depth_factor[None, :, None]
    levels = scaled_heat_values.shape[1]
    running = [scaled_heat_values[:, levels - 1]]
    for level in range(levels - 2, -1, -1):
        running.append(scaled_heat_values[:, level] + running[-1])
    partial_totals = jnp.stack(running[::-1], axis=1)
    lev_count = lax.axis_size("lev")
    bottom = running[-1]
    shifted = [lax.ppermute(bottom, "lev", [(d + k, d) for d in range(lev_count - k)])
               for k in range(1, lev_count)]
    deeper = shifted[0]
    for more in shifted[1:]:
        deeper = deeper + more
    geopotential = (partial_totals + deeper[:, None, :]).astype(jnp.bfloat16)
    return (values, geopotential)


def solution(mesh):
    return jax.shard_map(
        local,
        mesh=mesh,
        in_specs=(P("wave", None, "lev", None), P("wave", None, None, None), P(), P(), P()),
        out_specs=(P("wave", "lev", None), P("wave", "lev", None)),
        check_vma=False,
    )
```

```python
import jax
import jax.numpy as jnp
from jax import lax
from jax.sharding import PartitionSpec as P
from jax.experimental import pallas as pl
from jax.experimental.pallas import tpu as pltpu

TRUNC = 1279
QUANTITY_COUNT = 4
LCAP = 5248
BLOCK = 128
BLOCKS = LCAP // BLOCK
DEPTH = 48

two_pi = 6.283185307179586


def pair_masks(low_waves, pack_width):
    parity = jnp.arange(2, dtype=jnp.int32)
    low_count = (TRUNC - low_waves[:, None] - parity[None, :]) // 2 + 1
    high_count = (low_waves[:, None] - parity[None, :]) // 2 + 1
    pack_index = jnp.arange(pack_width, dtype=jnp.int32)[None, None, :]
    low_mask = pack_index < low_count[:, :, None]
    high_mask = (pack_index >= low_count[:, :, None]) & (
        pack_index < (low_count + high_count)[:, :, None]
    )
    return jnp.stack([low_mask, high_mask], axis=2)


def residue(j, points):
    q = jnp.floor(j.astype(jnp.float32) / points.astype(jnp.float32)).astype(jnp.int32)
    r = j - q * points
    r = jnp.where(r < 0, r + points, r)
    return jnp.where(r >= points, r - points, r)


def phase(waves, steps, points):
    j = waves * steps
    rem = residue(j, points)
    angle = rem.astype(jnp.float32) * (jnp.float32(two_pi) / points.astype(jnp.float32))
    return jnp.cos(angle), jnp.sin(angle)


def times(a, b):
    return a[0] * b[0] - a[1] * b[1], a[1] * b[0] + a[0] * b[1]


def tables(wave_numbers, lengths):
    w = wave_numbers[None, None, :]
    pts = lengths[:, None, None]
    low = phase(w, jnp.arange(16, dtype=jnp.int32)[None, :, None], pts)
    high = phase(w, 16 * jnp.arange(8, dtype=jnp.int32)[None, :, None], pts)
    near = phase(w, BLOCK * jnp.arange(8, dtype=jnp.int32)[None, :, None], pts)
    far = phase(w, 8 * BLOCK * jnp.arange(8, dtype=jnp.int32)[None, :, None], pts)
    wave_limit = jnp.minimum(TRUNC, (lengths - 1) // 2)
    keep = (wave_numbers[None, :] <= wave_limit[:, None]).astype(jnp.float32)[:, None, :]
    return jnp.concatenate(
        [low[0], low[1], high[0], high[1], near[0] * keep, near[1] * keep, far[0], far[1]], axis=1
    )


def expand(ph_ref, base_ref, tcos_ref, tsin_ref):
    slots = ph_ref.shape[2]
    p0c = ph_ref[0, 0:16, :]
    p0s = ph_ref[0, 16:32, :]
    for k1 in range(8):
        a = ph_ref[0, 32 + k1:33 + k1, :]
        b = ph_ref[0, 40 + k1:41 + k1, :]
        rows = slice(16 * k1, 16 * (k1 + 1))
        base_ref[rows, 0:slots] = (a * p0c - b * p0s).astype(jnp.bfloat16)
        base_ref[rows, slots:2 * slots] = (-(b * p0c + a * p0s)).astype(jnp.bfloat16)
    q0c = ph_ref[0, 48:56, :]
    q0s = ph_ref[0, 56:64, :]
    for b1 in range(6):
        a = ph_ref[0, 64 + b1:65 + b1, :]
        b = ph_ref[0, 72 + b1:73 + b1, :]
        rows = slice(8 * b1, 8 * (b1 + 1))
        tcos_ref[rows, :] = a * q0c - b * q0s
        tsin_ref[rows, :] = b * q0c + a * q0s


def main_kernel(lengths_ref, rowmap_ref, f_ref, ph_ref, out_ref, heat_ref, tw_ref, base_ref, cos_ref,
                sin_ref, kept_ref):
    expand(ph_ref, base_ref, cos_ref, sin_ref)
    r = pl.program_id(0)
    points = lengths_ref[r]
    fields = out_ref.shape[1]
    slots = f_ref.shape[2]
    real_part = f_ref[0, 0:fields, :]
    imag_part = f_ref[0, fields:2 * fields, :]
    for b in range(BLOCKS):
        c = cos_ref[b:b + 1, :]
        s = sin_ref[b:b + 1, :]
        rows = slice(fields * b, fields * (b + 1))
        tw_ref[rows, 0:slots] = (real_part * c - imag_part * s).astype(jnp.bfloat16)
        tw_ref[rows, slots:2 * slots] = (real_part * s + imag_part * c).astype(jnp.bfloat16)
    values = lax.dot_general(tw_ref[...], base_ref[...], (((1,), (1,)), ((), ())),
                             preferred_element_type=jnp.float32)
    lane = lax.broadcasted_iota(jnp.int32, (fields, BLOCK), 1)
    for b in range(BLOCKS):
        v = values[fields * b:fields * (b + 1), :]
        v = jnp.where(lane + BLOCK * b < points, v, 0.0).astype(jnp.bfloat16)
        out_ref[0, :, BLOCK * b:BLOCK * (b + 1)] = v
        kept_ref[fields * b:fields * (b + 1), :] = v.astype(jnp.float32)
    levels = heat_ref.shape[1]
    for level in range(levels):
        heat_ref[0, level] = kept_ref[pl.ds(QUANTITY_COUNT * level, BLOCKS, stride=fields), :]


def synth(fourier, ph, lengths, rowmap):
    rows, cols, slots = fourier.shape
    fields = cols // 2
    levels = fields // QUANTITY_COUNT
    grid_spec = pltpu.PrefetchScalarGridSpec(
        num_scalar_prefetch=2,
        grid=(rows,),
        in_specs=[
            pl.BlockSpec((1, cols, slots), lambda r, n, m: (m[r], 0, 0)),
            pl.BlockSpec((1, ph.shape[1], slots), lambda r, n, m: (r, 0, 0)),
        ],
        out_specs=[
            pl.BlockSpec((1, fields, LCAP), lambda r, n, m: (r, 0, 0)),
            pl.BlockSpec((1, levels, BLOCKS, BLOCK), lambda r, n, m: (r, 0, 0, 0)),
        ],
        scratch_shapes=[
            pltpu.VMEM((fields * BLOCKS, 2 * slots), jnp.bfloat16),
            pltpu.VMEM((BLOCK, 2 * slots), jnp.bfloat16),
            pltpu.VMEM((DEPTH, slots), jnp.float32),
            pltpu.VMEM((DEPTH, slots), jnp.float32),
            pltpu.VMEM((fields * BLOCKS, BLOCK), jnp.float32),
        ],
    )
    return pl.pallas_call(
        main_kernel,
        grid_spec=grid_spec,
        out_shape=(
            jax.ShapeDtypeStruct((rows, fields, LCAP), jnp.bfloat16),
            jax.ShapeDtypeStruct((rows, levels, BLOCKS, BLOCK), jnp.float32),
        ),
        compiler_params=pltpu.CompilerParams(dimension_semantics=("arbitrary",)),
    )(lengths, rowmap, fourier, ph)


def local(coefficients, legendre, pair_wave, row_points, layer_logpressure_factor):
    wave_count = lax.axis_size("wave")
    wave_rank = lax.axis_index("wave")
    pair_local, _, cols, pack_width = coefficients.shape
    fields = cols // 2
    half_rows = legendre.shape[3]
    all_rows = 2 * half_rows
    band_rows = all_rows // wave_count
    half_bands = half_rows // band_rows
    my_pairs = lax.dynamic_slice_in_dim(pair_wave, wave_rank * pair_local, pair_local)
    selection = pair_masks(my_pairs, pack_width).astype(jnp.bfloat16)
    coef = coefficients.reshape(pair_local, 2, fields, 2, pack_width).transpose(0, 1, 3, 2, 4)
    coef = coef.reshape(pair_local, 2, cols, pack_width)
    selected = coef[:, :, None, :, :] * selection[:, :, :, None, :]
    signs = jnp.array([[1.0, 1.0], [1.0, -1.0]], jnp.bfloat16)
    lhs = signs[None, :, :, None, None, None] * selected[:, None]
    sums = jnp.einsum("qaehci,qeit->atqhc", lhs, legendre, preferred_element_type=jnp.float32)
    sums = sums.reshape(2, half_bands, band_rows, pair_local, 2, cols)
    bands = jnp.concatenate([sums[0], jnp.flip(sums[1], 0)], 0)
    send = bands.transpose(0, 2, 3, 1, 4).reshape(wave_count, pair_local * 2, band_rows * cols)
    got = lax.all_to_all(send, "wave", 0, 0, tiled=True)
    slots = got.shape[0] * got.shape[1]
    fourier = got.reshape(slots, band_rows * cols).T.reshape(band_rows, cols, slots)
    south_side = (wave_rank >= half_bands).astype(jnp.int32)
    local_rows = jnp.arange(band_rows, dtype=jnp.int32)
    rowmap = local_rows + south_side * (band_rows - 1 - 2 * local_rows)

    wave_numbers = jnp.stack([pair_wave, TRUNC - pair_wave], axis=1).reshape(-1)
    points_all = jnp.concatenate([row_points, jnp.flip(row_points)])
    lengths = lax.dynamic_slice_in_dim(points_all, wave_rank * band_rows, band_rows)
    ph = tables(wave_numbers, lengths)
    values, heat = synth(fourier, ph, lengths, rowmap)
    heat_state_values = heat.reshape(band_rows, fields // QUANTITY_COUNT, LCAP)

    device_layers = heat_state_values.shape[1]
    lev_rank = lax.axis_index("lev")
    layer_depth_factor = lax.dynamic_slice_in_dim(
        layer_logpressure_factor, lev_rank * device_layers, device_layers
    )
    scaled_heat_values = heat_state_values * layer_depth_factor[None, :, None]
    levels = scaled_heat_values.shape[1]
    running = [scaled_heat_values[:, levels - 1]]
    for level in range(levels - 2, -1, -1):
        running.append(scaled_heat_values[:, level] + running[-1])
    partial_totals = jnp.stack(running[::-1], axis=1)
    lev_count = lax.axis_size("lev")
    bottom = running[-1]
    shifted = [lax.ppermute(bottom, "lev", [(d + k, d) for d in range(lev_count - k)])
               for k in range(1, lev_count)]
    deeper = shifted[0]
    for more in shifted[1:]:
        deeper = deeper + more
    geopotential = (partial_totals + deeper[:, None, :]).astype(jnp.bfloat16)
    return (values, geopotential)


def solution(mesh):
    return jax.shard_map(
        local,
        mesh=mesh,
        in_specs=(P("wave", None, "lev", None), P("wave", None, None, None), P(), P(), P()),
        out_specs=(P("wave", "lev", None), P("wave", "lev", None)),
        check_vma=False,
    )
```
